256 devices in a mesh: leaf: 32 (over x, z), basis: 2 (over core), coup: 4 (over y).
Axes of the slice: x: 4, y: 4, z: 8, core: 2. Of those that a mesh axis runs over, the one named last changes fastest.
Arguments:
- basis_rows: bfloat16 [2048, 131072], P('leaf', ('basis', 'coup')), may hold values from -0.125 to 0.125
- transfer: bfloat16 [3072, 4096], P('leaf'), may hold values from -0.5 to 0.5
- omega: bfloat16 [3584, 2048], P('leaf'), may hold values from -0.75 to 0.75
- blocks: bfloat16 [196608, 4096], P(('leaf', 'basis', 'coup')), may hold values from -6 to 6
- block_target: int32 [196608], P(('leaf', 'basis', 'coup')), may hold values from 0 to 111
- source_leaf: int32 [196608, 1], P(('leaf', 'basis', 'coup')), may hold values from 0 to 31; in each aligned block of 768 rows (0 to 767, 768 to 1535, ...) at most 36 rows name the same one
- source_offset: int32 [196608], P(('leaf', 'basis', 'coup')), may hold values from 0 to 63
Outputs:
- projected: float32 [196608, 1024], P(('leaf', 'basis', 'coup'))
The draws below stay inside these ranges and needn't reach their ends.
Inputs may be any that keep to these rules, and one draw needn't show every extreme that they name: `source_leaf`: among the 768 rows of one device, no branch is named by more than 36 rows, a bound that some block reaches.
All inputs are finite; a program needn't handle non-finite values.
Results may differ from the reference program's by a relative error of at most 0.0049.
Values may be sent and summed in bfloat16 or wider, within the bound.
No kernel may reach another device: no remote copies, remote signals or barrier semaphores. Data moves between devices by JAX's collectives and lax.ppermute only.
A program may use at most 128 MiB of HBM per device.

```python
import math
import jax
import jax.numpy as jnp
import numpy as np
from jax import lax

K = 64
R = 32
NB = 64
ROWS = 2048
B_DEV = 768
NPL = 112
CAP = 36
BLOCKS = 196608
BOTTOM = 2048
LINKED = 3072
NODES = 3584
N_LEAF = 32


def plant(array, stream_key, low, high):
    longest = array.shape.index(max(array.shape))
    spots = []
    for shift in (0, 1):
        where = [jax.random.randint(jax.random.fold_in(stream_key, axis), (), 0, length) for axis, length in enumerate(array.shape)]
        where[longest] = (where[longest] + shift) % array.shape[longest]
        spots.append(tuple(where))
    return array.at[spots[0]].set(low).at[spots[1]].set(high)


def shard_levels(key, shape, cuts, least, largest):
    loudness, own = 1.0, jax.random.fold_in(key, 6)
    for position, shards_of in cuts:
        steps = jnp.exp(jax.random.uniform(jax.random.fold_in(own, position), (shards_of,), jnp.float32, least / len(cuts), largest / len(cuts)))
        loudness = loudness * jnp.repeat(steps, shape[position] // shards_of).reshape([-1 if axis == position else 1 for axis in range(len(shape))])
    return loudness


def routed_block(own_key, own, number, rows, number_of, top, most, lean):
    order = jax.random.permutation(own_key, number_of)
    packed, ordinary = shares(number_of, rows * top, most, lean, True), shares(number_of, rows * top, most, lean, False)
    places = jnp.arange(number_of)

    def named(tallies, offset_by):
        used = int((tallies > 0).sum())
        fixed = max(1, used // 4)
        shifted = fixed + (places - fixed + offset_by * (used - fixed)) % max(1, number_of - fixed)
        return jnp.zeros((number_of,), jnp.int32).at[order[jnp.where(places < fixed, places, shifted)]].set(jnp.asarray(tallies, jnp.int32))

    tallies = jnp.where(number % 4 == 0, named(packed, number // 4), named(ordinary, number - number // 4 - 1))
    mixed = jax.random.permutation(jax.random.fold_in(own, 3), number_of)
    donor, sink = mixed[0:number_of // 2 * 2:2], mixed[1:number_of // 2 * 2:2]
    slack = jnp.minimum(tallies[donor] - 1, most - tallies[sink]) // 2
    slack = jnp.where((donor == order[0]) | (sink == order[0]) | (tallies[sink] == 0), 0, jnp.maximum(slack, 0))
    shifted = jax.random.randint(jax.random.fold_in(own, 4), (number_of // 2,), 0, 1 << 20) % (slack + 1)
    tallies = tallies.at[donor].add(-shifted).at[sink].add(shifted)
    items = jnp.searchsorted(jnp.cumsum(tallies), jnp.arange(rows * top), side="right").astype(jnp.int32)
    listing = items.reshape(top, rows).T
    listing = listing[jax.random.permutation(jax.random.fold_in(own, 1), rows)]
    offset_by = jax.random.randint(jax.random.fold_in(own, 2), (rows, 1), 0, top)
    return jnp.take_along_axis(listing, (jnp.arange(top)[None, :] + offset_by) % top, axis=1)


def shares(number_of, total, most, lean, full):
    loads = [(1 << 20) // math.isqrt(rank ** lean) + 1 for rank in range(1, number_of + 1)]
    largest = most if full else min(most, max(-(-total // number_of), total * loads[0] // sum(loads)))
    least = 1 if total - largest >= number_of - 1 else 0
    holding, spare = [largest] + [least] * (number_of - 1), total - largest - least * (number_of - 1)
    while spare > 0:
        candidates = [i for i in range(1, number_of) if holding[i] < largest] or [i for i in range(1, number_of) if holding[i] < most]
        whole, remaining = sum([loads[i] for i in candidates]), spare
        for i in candidates:
            more = min(most - holding[i], max(1, remaining * loads[i] // whole), spare)
            holding[i] = holding[i] + more
            spare = spare - more
    return np.array(holding)


def gaussian(stream_key, shape, spread, limit, cuts=(), kind=jnp.bfloat16):
    gain = shard_levels(stream_key, shape, cuts, -0.22, 0.18) if cuts else 1.0
    values = jax.random.normal(stream_key, shape, jnp.float32) * spread * gain
    return jnp.minimum(jnp.maximum(values, -limit), limit).astype(kind)


def setup_inputs(seed: int = 0) -> dict:
    arg_keys = jax.random.split(jax.random.key(seed), 8)
    basis_rows = gaussian(arg_keys[0], (BOTTOM, ROWS * K), ROWS ** -0.5, 0.125, ((0, 32), (1, 8)))
    transfer = gaussian(arg_keys[1], (LINKED, K * K), (2 * K) ** -0.5, 0.5, ((0, 32),))
    omega = gaussian(arg_keys[2], (NODES, K * R), K ** -0.5, 0.75, ((0, 32),))
    blocks = gaussian(arg_keys[3], (BLOCKS, K * K), 1.0, 6.0, ((0, 256),))
    block_target = plant(jax.random.randint(arg_keys[4], (BLOCKS,), 0, NPL), jax.random.fold_in(arg_keys[4], 1), 0, NPL - 1).astype(jnp.int32)
    source_leaf_keys = jax.random.split(jax.random.fold_in(arg_keys[5], 1), BLOCKS // B_DEV)
    source_leaf_turns = jax.random.permutation(jax.random.fold_in(arg_keys[5], 3), BLOCKS // B_DEV)
    source_leaf = jax.vmap(lambda own, number: routed_block(jax.random.fold_in(arg_keys[5], 2), own, number, B_DEV, N_LEAF, 1, CAP, 2))(source_leaf_keys, source_leaf_turns).reshape((BLOCKS, 1))
    source_offset = plant(jax.random.randint(arg_keys[6], (BLOCKS,), 0, NB), jax.random.fold_in(arg_keys[6], 1), 0, NB - 1).astype(jnp.int32)
    return dict(basis_rows=basis_rows, transfer=transfer, omega=omega, blocks=blocks, block_target=block_target, source_leaf=source_leaf, source_offset=source_offset)


def level_slots(target):
    base = jnp.where(target < NB, 0, jnp.where(target < NB + NB // 2, NB, NB + NB // 2))
    node_count = jnp.where(target < NB, NB, jnp.where(target < NB + NB // 2, NB // 2, NB // 4))
    return (base, node_count)

def upsweep(gram_bottom, transfer, omega):
    links = transfer.reshape(-1, K, K).astype(jnp.float32)
    levels = [gram_bottom]
    gram_now = gram_bottom
    offset_row = 0
    for node_count in (NB, NB // 2):
        child_links = links[offset_row:offset_row + node_count]
        offset_row = offset_row + node_count
        carried = jnp.einsum('nki,nkl,nlj->nij', child_links, gram_now, child_links, precision=lax.Precision.HIGHEST)
        gram_now = carried.reshape(node_count // 2, 2, K, K).sum(axis=1)
        levels.append(gram_now)
    gram_all = jnp.concatenate(levels, axis=0)
    factor = jnp.linalg.cholesky(gram_all)
    sketch = omega.reshape(-1, K, R).astype(jnp.float32)
    basis_table = jnp.einsum('nkr,njk->nrj', sketch, factor, precision=lax.Precision.HIGHEST)
    return basis_table.astype(jnp.bfloat16).reshape(-1, R * K)

def project(target_rows, source_rows, coupling):
    target_mat = target_rows.reshape(-1, R, K).astype(jnp.float32)
    coupling_mat = coupling.reshape(-1, K, K).astype(jnp.float32)
    left_prod = jnp.einsum('brk,bkl->brl', target_mat, coupling_mat).astype(jnp.bfloat16)
    source_mat = source_rows.reshape(-1, R, K).astype(jnp.float32)
    result = jnp.einsum('brl,bjl->brj', left_prod.astype(jnp.float32), source_mat)
    return result.reshape(-1, R * R)

def reference(basis_rows, transfer, omega, blocks, block_target, source_leaf, source_offset):
    rows_all = basis_rows.reshape(N_LEAF, NB, ROWS, K)
    links_all = transfer.reshape(N_LEAF, 3 * NB // 2, K * K)
    sketch_all = omega.reshape(N_LEAF, NPL, K * R)

    def one_leaf(items):
        rows_leaf, links_leaf, sketch_leaf = items
        widened = rows_leaf.astype(jnp.float32)
        gram_bottom = jnp.einsum('nik,nil->nkl', widened, widened, precision=lax.Precision.HIGHEST)
        return upsweep(gram_bottom, links_leaf, sketch_leaf)
    tables = lax.map(one_leaf, (rows_all, links_all, sketch_all))
    flat_table = tables.reshape(N_LEAF * NPL, R * K)
    group_size = BLOCKS // N_LEAF

    def one_group(items):
        leaf_id, coupling, target, src_leaf, offsets = items
        own_table = lax.dynamic_index_in_dim(tables, leaf_id, 0, keepdims=False)
        base, node_count = level_slots(target)
        global_id = src_leaf[:, 0] * NPL + base + offsets % node_count
        return project(own_table[target], flat_table[global_id], coupling)
    result = lax.map(one_group, (jnp.arange(N_LEAF, dtype=jnp.int32), blocks.reshape(N_LEAF, group_size, K * K), block_target.reshape(N_LEAF, group_size), source_leaf.reshape(N_LEAF, group_size, 1), source_offset.reshape(N_LEAF, group_size)))
    return result.reshape(BLOCKS, R * R)
```

```python
import jax
import jax.numpy as jnp
from jax import lax
from jax.sharding import PartitionSpec as P
from jax.experimental import pallas as pl
from jax.experimental.pallas import tpu as pltpu

K = 64
R = 32
NB = 64


def level_slots(target):
    base = jnp.where(target < NB, 0, jnp.where(target < NB + NB // 2, NB, NB + NB // 2))
    node_count = jnp.where(target < NB, NB, jnp.where(target < NB + NB // 2, NB // 2, NB // 4))
    return (base, node_count)


def upsweep(gram_bottom, transfer, omega, bottom_count):
    links = transfer.reshape(-1, K, K).astype(jnp.float32)
    levels = [gram_bottom]
    gram_now = gram_bottom
    offset_row = 0
    for node_count in (bottom_count, bottom_count // 2):
        child_links = links[offset_row : offset_row + node_count]
        offset_row = offset_row + node_count
        carried = jnp.einsum(
            "nki,nkl,nlj->nij", child_links, gram_now, child_links, precision=lax.Precision.HIGHEST
        )
        gram_now = carried.reshape(node_count // 2, 2, K, K).sum(axis=1)
        levels.append(gram_now)
    gram_all = jnp.concatenate(levels, axis=0)
    sketch_t = omega.reshape(-1, K, R).astype(jnp.float32).transpose(0, 2, 1)
    basis_table = chol_basis(gram_all, sketch_t)
    return basis_table.astype(jnp.bfloat16).reshape(-1, R * K)


def chol_kernel(g_ref, om_ref, out_ref, lt_ref):
    a = g_ref[...]
    count = a.shape[0]
    lane = lax.broadcasted_iota(jnp.int32, (count, 1, K), 2)
    for j in range(K):
        row = a[:, j : j + 1, :]
        inv = 1.0 / jnp.sqrt(row[:, :, j : j + 1])
        scaled = jnp.where(lane >= j, row * inv, 0.0)
        lt_ref[:, j : j + 1, :] = scaled
        col = a[:, :, j : j + 1] * inv
        a = a - col * scaled
    out_ref[...] = jnp.einsum(
        "nrk,nkj->nrj", om_ref[...], lt_ref[...], precision=lax.Precision.HIGHEST,
        preferred_element_type=jnp.float32,
    )


def chol_basis(gram_all, sketch_t):
    count = gram_all.shape[0]
    return pl.pallas_call(
        chol_kernel,
        out_shape=jax.ShapeDtypeStruct((count, R, K), jnp.float32),
        scratch_shapes=[pltpu.VMEM((count, K, K), jnp.float32)],
    )(gram_all, sketch_t)


def project(target_rows, source_rows, coupling):
    target_mat = target_rows.reshape(-1, R, K)
    coupling_mat = coupling.reshape(-1, K, K)
    left_prod = jnp.einsum(
        "brk,bkl->brl", target_mat, coupling_mat, preferred_element_type=jnp.float32
    ).astype(jnp.bfloat16)
    source_mat = source_rows.reshape(-1, R, K)
    result = jnp.einsum("brl,bjl->brj", left_prod, source_mat, preferred_element_type=jnp.float32)
    return result.reshape(-1, R * R)


def per_device(basis_rows, transfer, omega, blocks, block_target, source_leaf, source_offset):
    rows_local = basis_rows.reshape(NB, -1, K)
    partial_gram = jnp.einsum(
        "nik,nil->nkl", rows_local, rows_local, preferred_element_type=jnp.float32
    )
    gram_share = lax.psum_scatter(partial_gram, ("basis", "coup"), scatter_dimension=0, tiled=True)
    group = lax.axis_size(("basis", "coup"))
    member = lax.axis_index(("basis", "coup"))
    local_count = NB // group
    half_count = local_count // 2
    quarter_count = local_count // 4
    links_local = jnp.concatenate(
        [
            lax.dynamic_slice_in_dim(transfer, member * local_count, local_count, 0),
            lax.dynamic_slice_in_dim(transfer, NB + member * half_count, half_count, 0),
        ],
        axis=0,
    )
    sketch_local = jnp.concatenate(
        [
            lax.dynamic_slice_in_dim(omega, member * local_count, local_count, 0),
            lax.dynamic_slice_in_dim(omega, NB + member * half_count, half_count, 0),
            lax.dynamic_slice_in_dim(
                omega, NB + NB // 2 + member * quarter_count, quarter_count, 0
            ),
        ],
        axis=0,
    )
    local_table = upsweep(gram_share, links_local, sketch_local, local_count)
    collected = lax.all_gather(local_table, ("basis", "coup"), axis=0, tiled=True)
    collected = collected.reshape(group, local_count + half_count + quarter_count, R * K)
    basis_table = jnp.concatenate(
        [
            collected[:, :local_count].reshape(-1, R * K),
            collected[:, local_count : local_count + half_count].reshape(-1, R * K),
            collected[:, local_count + half_count :].reshape(-1, R * K),
        ],
        axis=0,
    )
    slots_per_leaf = basis_table.shape[0]
    base, node_count = level_slots(block_target)
    source_slot = base + source_offset % node_count
    source_peer = source_leaf[:, 0]
    gathered = lax.all_gather(basis_table, "leaf", axis=0, tiled=True)
    source_rows = gathered[source_peer * slots_per_leaf + source_slot]
    return project(basis_table[block_target], source_rows, blocks)


def solution(mesh):
    placed = (
        P("leaf", ("basis", "coup")),
        P("leaf", None),
        P("leaf", None),
        P(("leaf", "basis", "coup"), None),
        P(("leaf", "basis", "coup")),
        P(("leaf", "basis", "coup"), None),
        P(("leaf", "basis", "coup")),
    )
    return jax.shard_map(
        per_device,
        mesh=mesh,
        in_specs=placed,
        out_specs=P(("leaf", "basis", "coup"), None),
        check_vma=False,
    )
```

```python
import jax
import jax.numpy as jnp
from jax import lax
from jax.sharding import PartitionSpec as P
from jax.experimental import pallas as pl
from jax.experimental.pallas import tpu as pltpu

K = 64
R = 32
NB = 64


def level_slots(target):
    base = jnp.where(target < NB, 0, jnp.where(target < NB + NB // 2, NB, NB + NB // 2))
    node_count = jnp.where(target < NB, NB, jnp.where(target < NB + NB // 2, NB // 2, NB // 4))
    return (base, node_count)


def upsweep(gram_bottom, transfer, omega, bottom_count):
    links = transfer.reshape(-1, K, K).astype(jnp.float32)
    levels = [gram_bottom]
    gram_now = gram_bottom
    offset_row = 0
    for node_count in (bottom_count, bottom_count // 2):
        child_links = links[offset_row : offset_row + node_count]
        offset_row = offset_row + node_count
        carried = jnp.einsum(
            "nki,nkl,nlj->nij", child_links, gram_now, child_links, precision=lax.Precision.HIGHEST
        )
        gram_now = carried.reshape(node_count // 2, 2, K, K).sum(axis=1)
        levels.append(gram_now)
    gram_all = jnp.concatenate(levels, axis=0)
    sketch_t = omega.reshape(-1, K, R).astype(jnp.float32).transpose(0, 2, 1)
    basis_table = chol_basis(gram_all, sketch_t)
    return basis_table.astype(jnp.bfloat16).reshape(-1, R * K)


def chol_kernel(g_ref, om_ref, out_ref, lt_ref):
    a = g_ref[...]
    count = a.shape[0]
    lane = lax.broadcasted_iota(jnp.int32, (count, 1, K), 2)
    for j in range(K):
        row = a[:, j : j + 1, :]
        inv = 1.0 / jnp.sqrt(row[:, :, j : j + 1])
        scaled = jnp.where(lane >= j, row * inv, 0.0)
        lt_ref[:, j : j + 1, :] = scaled
        col = a[:, :, j : j + 1] * inv
        a = a - col * scaled
    out_ref[...] = jnp.einsum(
        "nrk,nkj->nrj", om_ref[...], lt_ref[...], precision=lax.Precision.HIGHEST,
        preferred_element_type=jnp.float32,
    )


def chol_basis(gram_all, sketch_t):
    count = gram_all.shape[0]
    return pl.pallas_call(
        chol_kernel,
        out_shape=jax.ShapeDtypeStruct((count, R, K), jnp.float32),
        scratch_shapes=[pltpu.VMEM((count, K, K), jnp.float32)],
    )(gram_all, sketch_t)


def project(target_rows, source_rows, coupling):
    target_mat = target_rows.reshape(-1, R, K)
    coupling_mat = coupling.reshape(-1, K, K)
    left_prod = jnp.einsum(
        "brk,bkl->brl", target_mat, coupling_mat, preferred_element_type=jnp.float32
    ).astype(jnp.bfloat16)
    source_mat = source_rows.reshape(-1, R, K)
    result = jnp.einsum("brl,bjl->brj", left_prod, source_mat, preferred_element_type=jnp.float32)
    return result.reshape(-1, R * R)


def per_device(basis_rows, transfer, omega, blocks, block_target, source_leaf, source_offset):
    rows_local = basis_rows.reshape(NB, -1, K)
    partial_gram = jnp.einsum(
        "nik,nil->nkl", rows_local, rows_local, preferred_element_type=jnp.float32
    )
    gram_share = lax.psum_scatter(partial_gram, ("basis", "coup"), scatter_dimension=0, tiled=True)
    group = lax.axis_size(("basis", "coup"))
    member = lax.axis_index(("basis", "coup"))
    local_count = NB // group
    half_count = local_count // 2
    quarter_count = local_count // 4
    links_local = jnp.concatenate(
        [
            lax.dynamic_slice_in_dim(transfer, member * local_count, local_count, 0),
            lax.dynamic_slice_in_dim(transfer, NB + member * half_count, half_count, 0),
        ],
        axis=0,
    )
    sketch_local = jnp.concatenate(
        [
            lax.dynamic_slice_in_dim(omega, member * local_count, local_count, 0),
            lax.dynamic_slice_in_dim(omega, NB + member * half_count, half_count, 0),
            lax.dynamic_slice_in_dim(
                omega, NB + NB // 2 + member * quarter_count, quarter_count, 0
            ),
        ],
        axis=0,
    )
    local_table = upsweep(gram_share, links_local, sketch_local, local_count)
    collected = lax.all_gather(local_table, ("basis", "coup"), axis=0, tiled=True)
    collected = collected.reshape(group, local_count + half_count + quarter_count, R * K)
    basis_table = jnp.concatenate(
        [
            collected[:, :local_count].reshape(-1, R * K),
            collected[:, local_count : local_count + half_count].reshape(-1, R * K),
            collected[:, local_count + half_count :].reshape(-1, R * K),
        ],
        axis=0,
    )
    slots_per_leaf = basis_table.shape[0]
    base, node_count = level_slots(block_target)
    source_slot = base + source_offset % node_count
    source_peer = source_leaf[:, 0]
    half_slots = slots_per_leaf // 2
    core = lax.axis_index("basis")
    own_half = lax.dynamic_slice_in_dim(basis_table, core * half_slots, half_slots, 0)
    gathered = lax.all_gather(own_half, "leaf", axis=0, tiled=True)
    gathered = lax.all_gather(gathered, "basis", axis=0, tiled=True)
    leaves = lax.axis_size("leaf")
    source_index = (
        (source_slot // half_slots) * (leaves * half_slots)
        + source_peer * half_slots
        + source_slot % half_slots
    )
    source_rows = gathered[source_index]
    return project(basis_table[block_target], source_rows, blocks)


def solution(mesh):
    placed = (
        P("leaf", ("basis", "coup")),
        P("leaf", None),
        P("leaf", None),
        P(("leaf", "basis", "coup"), None),
        P(("leaf", "basis", "coup")),
        P(("leaf", "basis", "coup"), None),
        P(("leaf", "basis", "coup")),
    )
    return jax.shard_map(
        per_device,
        mesh=mesh,
        in_specs=placed,
        out_specs=P(("leaf", "basis", "coup"), None),
        check_vma=False,
    )
```

```python
import jax
import jax.numpy as jnp
from jax import lax
from jax.sharding import PartitionSpec as P
from jax.experimental import pallas as pl
from jax.experimental.pallas import tpu as pltpu

K = 64
R = 32
NB = 64


def level_slots(target):
    base = jnp.where(target < NB, 0, jnp.where(target < NB + NB // 2, NB, NB + NB // 2))
    node_count = jnp.where(target < NB, NB, jnp.where(target < NB + NB // 2, NB // 2, NB // 4))
    return (base, node_count)


def upsweep(gram_bottom, transfer, omega, bottom_count):
    links = transfer.reshape(-1, K, K).astype(jnp.float32)
    levels = [gram_bottom]
    gram_now = gram_bottom
    offset_row = 0
    for node_count in (bottom_count, bottom_count // 2):
        child_links = links[offset_row : offset_row + node_count]
        offset_row = offset_row + node_count
        carried = jnp.einsum(
            "nki,nkl,nlj->nij", child_links, gram_now, child_links, precision=lax.Precision.HIGHEST
        )
        gram_now = carried.reshape(node_count // 2, 2, K, K).sum(axis=1)
        levels.append(gram_now)
    gram_all = jnp.concatenate(levels, axis=0)
    sketch_t = omega.reshape(-1, K, R).astype(jnp.float32).transpose(0, 2, 1)
    basis_table = chol_basis(gram_all, sketch_t)
    return basis_table.astype(jnp.bfloat16).reshape(-1, R * K)


def chol_kernel(g_ref, om_ref, out_ref, lt_ref):
    a = g_ref[...]
    count = a.shape[0]
    lane = lax.broadcasted_iota(jnp.int32, (count, 1, K), 2)
    for j in range(K):
        row = a[:, j : j + 1, :]
        inv = 1.0 / jnp.sqrt(row[:, :, j : j + 1])
        scaled = jnp.where(lane >= j, row * inv, 0.0)
        lt_ref[:, j : j + 1, :] = scaled
        col = a[:, :, j : j + 1] * inv
        a = a - col * scaled
    out_ref[...] = jnp.einsum(
        "nrk,nkj->nrj", om_ref[...], lt_ref[...], precision=lax.Precision.HIGHEST,
        preferred_element_type=jnp.float32,
    )


def chol_basis(gram_all, sketch_t):
    count = gram_all.shape[0]
    return pl.pallas_call(
        chol_kernel,
        out_shape=jax.ShapeDtypeStruct((count, R, K), jnp.float32),
        scratch_shapes=[pltpu.VMEM((count, K, K), jnp.float32)],
    )(gram_all, sketch_t)


def project_kernel(t_ref, s_ref, src_ref, o_ref):
    tile = t_ref.shape[0]
    target_mat = t_ref[...].reshape(tile, R, K)
    coupling_mat = s_ref[...].reshape(tile, K, K)
    source_mat = src_ref[...].reshape(tile, R, K)
    left_prod = jnp.einsum(
        "brk,bkl->brl", target_mat, coupling_mat, preferred_element_type=jnp.float32
    ).astype(jnp.bfloat16)
    result = jnp.einsum("brl,bjl->brj", left_prod, source_mat, preferred_element_type=jnp.float32)
    o_ref[...] = result.reshape(tile, R * R)


def project(target_rows, source_rows, coupling):
    count = coupling.shape[0]
    tile = 128 if count % 128 == 0 else count
    return pl.pallas_call(
        project_kernel,
        grid=(count // tile,),
        in_specs=[
            pl.BlockSpec((tile, R * K), lambda i: (i, 0)),
            pl.BlockSpec((tile, K * K), lambda i: (i, 0)),
            pl.BlockSpec((tile, R * K), lambda i: (i, 0)),
        ],
        out_specs=pl.BlockSpec((tile, R * R), lambda i: (i, 0)),
        out_shape=jax.ShapeDtypeStruct((count, R * R), jnp.float32),
    )(target_rows, coupling, source_rows)


def per_device(basis_rows, transfer, omega, blocks, block_target, source_leaf, source_offset):
    rows_local = basis_rows.reshape(NB, -1, K)
    partial_gram = jnp.einsum(
        "nik,nil->nkl", rows_local, rows_local, preferred_element_type=jnp.float32
    )
    gram_share = lax.psum_scatter(partial_gram, ("basis", "coup"), scatter_dimension=0, tiled=True)
    group = lax.axis_size(("basis", "coup"))
    member = lax.axis_index(("basis", "coup"))
    local_count = NB // group
    half_count = local_count // 2
    quarter_count = local_count // 4
    links_local = jnp.concatenate(
        [
            lax.dynamic_slice_in_dim(transfer, member * local_count, local_count, 0),
            lax.dynamic_slice_in_dim(transfer, NB + member * half_count, half_count, 0),
        ],
        axis=0,
    )
    sketch_local = jnp.concatenate(
        [
            lax.dynamic_slice_in_dim(omega, member * local_count, local_count, 0),
            lax.dynamic_slice_in_dim(omega, NB + member * half_count, half_count, 0),
            lax.dynamic_slice_in_dim(
                omega, NB + NB // 2 + member * quarter_count, quarter_count, 0
            ),
        ],
        axis=0,
    )
    local_table = upsweep(gram_share, links_local, sketch_local, local_count)
    collected = lax.all_gather(local_table, ("basis", "coup"), axis=0, tiled=True)
    collected = collected.reshape(group, local_count + half_count + quarter_count, R * K)
    basis_table = jnp.concatenate(
        [
            collected[:, :local_count].reshape(-1, R * K),
            collected[:, local_count : local_count + half_count].reshape(-1, R * K),
            collected[:, local_count + half_count :].reshape(-1, R * K),
        ],
        axis=0,
    )
    slots_per_leaf = basis_table.shape[0]
    base, node_count = level_slots(block_target)
    source_slot = base + source_offset % node_count
    source_peer = source_leaf[:, 0]
    gathered = lax.all_gather(basis_table, "leaf", axis=0, tiled=True)
    source_rows = gathered[source_peer * slots_per_leaf + source_slot]
    return project(basis_table[block_target], source_rows, blocks)


def solution(mesh):
    placed = (
        P("leaf", ("basis", "coup")),
        P("leaf", None),
        P("leaf", None),
        P(("leaf", "basis", "coup"), None),
        P(("leaf", "basis", "coup")),
        P(("leaf", "basis", "coup"), None),
        P(("leaf", "basis", "coup")),
    )
    return jax.shard_map(
        per_device,
        mesh=mesh,
        in_specs=placed,
        out_specs=P(("leaf", "basis", "coup"), None),
        check_vma=False,
    )
```

```python
import jax
import jax.numpy as jnp
from jax import lax
from jax.sharding import PartitionSpec as P
from jax.experimental import pallas as pl
from jax.experimental.pallas import tpu as pltpu

K = 64
R = 32
NB = 64


def level_slots(target):
    base = jnp.where(target < NB, 0, jnp.where(target < NB + NB // 2, NB, NB + NB // 2))
    node_count = jnp.where(target < NB, NB, jnp.where(target < NB + NB // 2, NB // 2, NB // 4))
    return (base, node_count)


def upsweep(gram_bottom, transfer, omega, bottom_count):
    links = transfer.reshape(-1, K, K).astype(jnp.float32)
    levels = [gram_bottom]
    gram_now = gram_bottom
    offset_row = 0
    for node_count in (bottom_count, bottom_count // 2):
        child_links = links[offset_row : offset_row + node_count]
        offset_row = offset_row + node_count
        carried = jnp.einsum(
            "nki,nkl,nlj->nij", child_links, gram_now, child_links, precision=lax.Precision.HIGHEST
        )
        gram_now = carried.reshape(node_count // 2, 2, K, K).sum(axis=1)
        levels.append(gram_now)
    gram_all = jnp.concatenate(levels, axis=0)
    sketch_t = omega.reshape(-1, K, R).astype(jnp.float32).transpose(0, 2, 1)
    basis_table = chol_basis(gram_all, sketch_t)
    return basis_table.astype(jnp.bfloat16).reshape(-1, R * K)


def chol_kernel(g_ref, om_ref, out_ref, lt_ref):
    a = g_ref[...]
    count = a.shape[0]
    lane = lax.broadcasted_iota(jnp.int32, (count, 1, K), 2)
    for j in range(K):
        row = a[:, j : j + 1, :]
        inv = 1.0 / jnp.sqrt(row[:, :, j : j + 1])
        scaled = jnp.where(lane >= j, row * inv, 0.0)
        lt_ref[:, j : j + 1, :] = scaled
        col = a[:, :, j : j + 1] * inv
        a = a - col * scaled
    out_ref[...] = jnp.einsum(
        "nrk,nkj->nrj", om_ref[...], lt_ref[...], precision=lax.Precision.HIGHEST,
        preferred_element_type=jnp.float32,
    )


def chol_basis(gram_all, sketch_t):
    count = gram_all.shape[0]
    return pl.pallas_call(
        chol_kernel,
        out_shape=jax.ShapeDtypeStruct((count, R, K), jnp.float32),
        scratch_shapes=[pltpu.VMEM((count, K, K), jnp.float32)],
    )(gram_all, sketch_t)


def project_kernel(t_ref, s_ref, src_ref, o_ref):
    tile = t_ref.shape[0]
    target_mat = t_ref[...].reshape(tile, R, K)
    coupling_mat = s_ref[...].reshape(tile, K, K)
    source_mat = src_ref[...].reshape(tile, R, K)
    left_prod = jnp.einsum(
        "brk,bkl->brl", target_mat, coupling_mat, preferred_element_type=jnp.float32
    ).astype(jnp.bfloat16)
    result = jnp.einsum("brl,bjl->brj", left_prod, source_mat, preferred_element_type=jnp.float32)
    o_ref[...] = result.reshape(tile, R * R)


def project(target_rows, source_rows, coupling):
    count = coupling.shape[0]
    tile = 128 if count % 128 == 0 else count
    return pl.pallas_call(
        project_kernel,
        grid=(count // tile,),
        in_specs=[
            pl.BlockSpec((tile, R * K), lambda i: (i, 0)),
            pl.BlockSpec((tile, K * K), lambda i: (i, 0)),
            pl.BlockSpec((tile, R * K), lambda i: (i, 0)),
        ],
        out_specs=pl.BlockSpec((tile, R * R), lambda i: (i, 0)),
        out_shape=jax.ShapeDtypeStruct((count, R * R), jnp.float32),
    )(target_rows, coupling, source_rows)


def per_device(basis_rows, transfer, omega, blocks, block_target, source_leaf, source_offset):
    rows_local = basis_rows.reshape(NB, -1, K)
    partial_gram = jnp.einsum(
        "nik,nil->nkl", rows_local, rows_local, preferred_element_type=jnp.float32
    )
    gram_share = lax.psum_scatter(partial_gram, ("basis", "coup"), scatter_dimension=0, tiled=True)
    group = lax.axis_size(("basis", "coup"))
    member = lax.axis_index(("basis", "coup"))
    local_count = NB // group
    half_count = local_count // 2
    quarter_count = local_count // 4
    links_local = jnp.concatenate(
        [
            lax.dynamic_slice_in_dim(transfer, member * local_count, local_count, 0),
            lax.dynamic_slice_in_dim(transfer, NB + member * half_count, half_count, 0),
        ],
        axis=0,
    )
    sketch_local = jnp.concatenate(
        [
            lax.dynamic_slice_in_dim(omega, member * local_count, local_count, 0),
            lax.dynamic_slice_in_dim(omega, NB + member * half_count, half_count, 0),
            lax.dynamic_slice_in_dim(
                omega, NB + NB // 2 + member * quarter_count, quarter_count, 0
            ),
        ],
        axis=0,
    )
    local_table = upsweep(gram_share, links_local, sketch_local, local_count)
    collected = lax.all_gather(local_table, ("basis", "coup"), axis=0, tiled=True)
    collected = collected.reshape(group, local_count + half_count + quarter_count, R * K)
    basis_table = jnp.concatenate(
        [
            collected[:, :local_count].reshape(-1, R * K),
            collected[:, local_count : local_count + half_count].reshape(-1, R * K),
            collected[:, local_count + half_count :].reshape(-1, R * K),
        ],
        axis=0,
    )
    slots_per_leaf = basis_table.shape[0]
    local_rows = local_table.shape[0]
    base, node_count = level_slots(block_target)
    within = source_offset % node_count
    per_member = node_count // group
    source_member = source_leaf[:, 0] * group + within // per_member
    source_index = source_member * local_rows + base // group + within % per_member
    gathered = lax.all_gather(local_table, ("leaf", "basis", "coup"), axis=0, tiled=True)
    source_rows = gathered[source_index]
    return project(basis_table[block_target], source_rows, blocks)


def solution(mesh):
    placed = (
        P("leaf", ("basis", "coup")),
        P("leaf", None),
        P("leaf", None),
        P(("leaf", "basis", "coup"), None),
        P(("leaf", "basis", "coup")),
        P(("leaf", "basis", "coup"), None),
        P(("leaf", "basis", "coup")),
    )
    return jax.shard_map(
        per_device,
        mesh=mesh,
        in_specs=placed,
        out_specs=P(("leaf", "basis", "coup"), None),
        check_vma=False,
    )
```

```python
import jax
import jax.numpy as jnp
from jax import lax
from jax.sharding import PartitionSpec as P
from jax.experimental import pallas as pl
from jax.experimental.pallas import tpu as pltpu

K = 64
R = 32
NB = 64


def level_slots(target):
    base = jnp.where(target < NB, 0, jnp.where(target < NB + NB // 2, NB, NB + NB // 2))
    node_count = jnp.where(target < NB, NB, jnp.where(target < NB + NB // 2, NB // 2, NB // 4))
    return (base, node_count)


def upsweep(gram_bottom, transfer, omega, bottom_count):
    links = transfer.reshape(-1, K, K).astype(jnp.float32)
    levels = [gram_bottom]
    gram_now = gram_bottom
    offset_row = 0
    for node_count in (bottom_count, bottom_count // 2):
        child_links = links[offset_row : offset_row + node_count]
        offset_row = offset_row + node_count
        carried = jnp.einsum(
            "nki,nkl,nlj->nij", child_links, gram_now, child_links, precision=lax.Precision.HIGHEST
        )
        gram_now = carried.reshape(node_count // 2, 2, K, K).sum(axis=1)
        levels.append(gram_now)
    gram_all = jnp.concatenate(levels, axis=0)
    sketch_t = omega.reshape(-1, K, R).astype(jnp.float32).transpose(0, 2, 1)
    basis_table = chol_basis(gram_all, sketch_t)
    return basis_table.astype(jnp.bfloat16).reshape(-1, R * K)


def chol_kernel(g_ref, om_ref, out_ref, lt_ref):
    a = g_ref[...]
    count = a.shape[0]
    lane = lax.broadcasted_iota(jnp.int32, (count, 1, K), 2)
    for j in range(K):
        row = a[:, j : j + 1, :]
        inv = 1.0 / jnp.sqrt(row[:, :, j : j + 1])
        scaled = jnp.where(lane >= j, row * inv, 0.0)
        lt_ref[:, j : j + 1, :] = scaled
        col = a[:, :, j : j + 1] * inv
        a = a - col * scaled
    out_ref[...] = jnp.einsum(
        "nrk,nkj->nrj", om_ref[...], lt_ref[...], precision=lax.Precision.HIGHEST,
        preferred_element_type=jnp.float32,
    )


def chol_basis(gram_all, sketch_t):
    count = gram_all.shape[0]
    return pl.pallas_call(
        chol_kernel,
        out_shape=jax.ShapeDtypeStruct((count, R, K), jnp.float32),
        scratch_shapes=[pltpu.VMEM((count, K, K), jnp.float32)],
    )(gram_all, sketch_t)


def left_kernel(t_ref, s_ref, o_ref):
    tile = t_ref.shape[0]
    target_mat = t_ref[...].reshape(tile, R, K)
    coupling_mat = s_ref[...].reshape(tile, K, K)
    left_prod = jnp.einsum(
        "brk,bkl->brl", target_mat, coupling_mat, preferred_element_type=jnp.float32
    )
    o_ref[...] = left_prod.astype(jnp.bfloat16).reshape(tile, R * K)


def right_kernel(l_ref, src_ref, o_ref):
    tile = l_ref.shape[0]
    left_prod = l_ref[...].reshape(tile, R, K)
    source_mat = src_ref[...].reshape(tile, R, K)
    result = jnp.einsum("brl,bjl->brj", left_prod, source_mat, preferred_element_type=jnp.float32)
    o_ref[...] = result.reshape(tile, R * R)


def row_tiled(kernel, widths, out_width, out_dtype, *arrays):
    count = arrays[0].shape[0]
    tile = 128 if count % 128 == 0 else count
    return pl.pallas_call(
        kernel,
        grid=(count // tile,),
        in_specs=[pl.BlockSpec((tile, w), lambda i: (i, 0)) for w in widths],
        out_specs=pl.BlockSpec((tile, out_width), lambda i: (i, 0)),
        out_shape=jax.ShapeDtypeStruct((count, out_width), out_dtype),
    )(*arrays)


def left_product(target_rows, coupling):
    return row_tiled(left_kernel, (R * K, K * K), R * K, jnp.bfloat16, target_rows, coupling)


def right_product(left_rows, source_rows):
    return row_tiled(right_kernel, (R * K, R * K), R * R, jnp.float32, left_rows, source_rows)


def per_device(basis_rows, transfer, omega, blocks, block_target, source_leaf, source_offset):
    rows_local = basis_rows.reshape(NB, -1, K)
    partial_gram = jnp.einsum(
        "nik,nil->nkl", rows_local, rows_local, preferred_element_type=jnp.float32
    )
    gram_share = lax.psum_scatter(partial_gram, ("basis", "coup"), scatter_dimension=0, tiled=True)
    group = lax.axis_size(("basis", "coup"))
    member = lax.axis_index(("basis", "coup"))
    local_count = NB // group
    half_count = local_count // 2
    quarter_count = local_count // 4
    links_local = jnp.concatenate(
        [
            lax.dynamic_slice_in_dim(transfer, member * local_count, local_count, 0),
            lax.dynamic_slice_in_dim(transfer, NB + member * half_count, half_count, 0),
        ],
        axis=0,
    )
    sketch_local = jnp.concatenate(
        [
            lax.dynamic_slice_in_dim(omega, member * local_count, local_count, 0),
            lax.dynamic_slice_in_dim(omega, NB + member * half_count, half_count, 0),
            lax.dynamic_slice_in_dim(
                omega, NB + NB // 2 + member * quarter_count, quarter_count, 0
            ),
        ],
        axis=0,
    )
    local_table = upsweep(gram_share, links_local, sketch_local, local_count)
    collected = lax.all_gather(local_table, ("basis", "coup"), axis=0, tiled=True)
    collected = collected.reshape(group, local_count + half_count + quarter_count, R * K)
    basis_table = jnp.concatenate(
        [
            collected[:, :local_count].reshape(-1, R * K),
            collected[:, local_count : local_count + half_count].reshape(-1, R * K),
            collected[:, local_count + half_count :].reshape(-1, R * K),
        ],
        axis=0,
    )
    slots_per_leaf = basis_table.shape[0]
    left_rows = left_product(basis_table[block_target], blocks)
    local_rows = -(-local_table.shape[0] // 8) * 8
    padded_table = jnp.pad(local_table, ((0, local_rows - local_table.shape[0]), (0, 0)))
    base, node_count = level_slots(block_target)
    within = source_offset % node_count
    per_member = node_count // group
    source_member = source_leaf[:, 0] * group + within // per_member
    source_index = source_member * local_rows + base // group + within % per_member
    gathered = lax.all_gather(padded_table, ("leaf", "basis", "coup"), axis=0, tiled=True)
    source_rows = gathered[source_index]
    return right_product(left_rows, source_rows)


def solution(mesh):
    placed = (
        P("leaf", ("basis", "coup")),
        P("leaf", None),
        P("leaf", None),
        P(("leaf", "basis", "coup"), None),
        P(("leaf", "basis", "coup")),
        P(("leaf", "basis", "coup"), None),
        P(("leaf", "basis", "coup")),
    )
    return jax.shard_map(
        per_device,
        mesh=mesh,
        in_specs=placed,
        out_specs=P(("leaf", "basis", "coup"), None),
        check_vma=False,
    )
```

```python
import jax
import jax.numpy as jnp
from jax import lax
from jax.sharding import PartitionSpec as P
from jax.experimental import pallas as pl
from jax.experimental.pallas import tpu as pltpu

K = 64
R = 32
NB = 64


def level_slots(target):
    base = jnp.where(target < NB, 0, jnp.where(target < NB + NB // 2, NB, NB + NB // 2))
    node_count = jnp.where(target < NB, NB, jnp.where(target < NB + NB // 2, NB // 2, NB // 4))
    return (base, node_count)


def upsweep(gram_bottom, transfer, omega, bottom_count):
    links = transfer.reshape(-1, K, K).astype(jnp.float32)
    levels = [gram_bottom]
    gram_now = gram_bottom
    offset_row = 0
    for node_count in (bottom_count, bottom_count // 2):
        child_links = links[offset_row : offset_row + node_count]
        offset_row = offset_row + node_count
        carried = jnp.einsum(
            "nki,nkl,nlj->nij", child_links, gram_now, child_links, precision=lax.Precision.HIGHEST
        )
        gram_now = carried.reshape(node_count // 2, 2, K, K).sum(axis=1)
        levels.append(gram_now)
    gram_all = jnp.concatenate(levels, axis=0)
    sketch_t = omega.reshape(-1, K, R).astype(jnp.float32).transpose(0, 2, 1)
    basis_table = chol_basis(gram_all, sketch_t)
    return basis_table.astype(jnp.bfloat16).reshape(-1, R * K)


def chol_kernel(g_ref, om_ref, out_ref, lt_ref):
    a = g_ref[...]
    count = a.shape[0]
    lane = lax.broadcasted_iota(jnp.int32, (count, 1, K), 2)
    for j in range(K):
        row = a[:, j : j + 1, :]
        inv = 1.0 / jnp.sqrt(row[:, :, j : j + 1])
        scaled = jnp.where(lane >= j, row * inv, 0.0)
        lt_ref[:, j : j + 1, :] = scaled
        col = a[:, :, j : j + 1] * inv
        a = a - col * scaled
    out_ref[...] = jnp.einsum(
        "nrk,nkj->nrj", om_ref[...], lt_ref[...], precision=lax.Precision.HIGHEST,
        preferred_element_type=jnp.float32,
    )


def chol_basis(gram_all, sketch_t):
    count = gram_all.shape[0]
    return pl.pallas_call(
        chol_kernel,
        out_shape=jax.ShapeDtypeStruct((count, R, K), jnp.float32),
        scratch_shapes=[pltpu.VMEM((count, K, K), jnp.float32)],
    )(gram_all, sketch_t)


def left_kernel(t_ref, s_ref, o_ref):
    tile = t_ref.shape[0]
    target_mat = t_ref[...].reshape(tile, R, K)
    coupling_mat = s_ref[...].reshape(tile, K, K)
    left_prod = jnp.einsum(
        "brk,bkl->brl", target_mat, coupling_mat, preferred_element_type=jnp.float32
    )
    o_ref[...] = left_prod.astype(jnp.bfloat16).reshape(tile, R * K)


def right_kernel(l_ref, src_ref, o_ref):
    tile = l_ref.shape[0]
    left_prod = l_ref[...].reshape(tile, R, K)
    source_mat = src_ref[...].reshape(tile, R, K)
    result = jnp.einsum("brl,bjl->brj", left_prod, source_mat, preferred_element_type=jnp.float32)
    o_ref[...] = result.reshape(tile, R * R)


def row_tiled(kernel, widths, out_width, out_dtype, *arrays):
    count = arrays[0].shape[0]
    tile = 128 if count % 128 == 0 else count
    return pl.pallas_call(
        kernel,
        grid=(count // tile,),
        in_specs=[pl.BlockSpec((tile, w), lambda i: (i, 0)) for w in widths],
        out_specs=pl.BlockSpec((tile, out_width), lambda i: (i, 0)),
        out_shape=jax.ShapeDtypeStruct((count, out_width), out_dtype),
    )(*arrays)


def left_product(target_rows, coupling):
    return row_tiled(left_kernel, (R * K, K * K), R * K, jnp.bfloat16, target_rows, coupling)


def right_product(left_rows, source_rows):
    return row_tiled(right_kernel, (R * K, R * K), R * R, jnp.float32, left_rows, source_rows)


def gram_kernel(x_ref, o_ref):
    tile = x_ref.shape[0]
    rows = x_ref[...].reshape(tile, -1, K)
    o_ref[...] = jnp.einsum("nik,nil->nkl", rows, rows, preferred_element_type=jnp.float32)


def local_gram(basis_rows):
    count, width = basis_rows.shape
    tile = 32 if count % 32 == 0 else count
    return pl.pallas_call(
        gram_kernel,
        grid=(count // tile,),
        in_specs=[pl.BlockSpec((tile, width), lambda i: (i, 0))],
        out_specs=pl.BlockSpec((tile, K, K), lambda i: (i, 0, 0)),
        out_shape=jax.ShapeDtypeStruct((count, K, K), jnp.float32),
    )(basis_rows)


def per_device(basis_rows, transfer, omega, blocks, block_target, source_leaf, source_offset):
    partial_gram = local_gram(basis_rows)
    gram_share = lax.psum_scatter(partial_gram, ("basis", "coup"), scatter_dimension=0, tiled=True)
    group = lax.axis_size(("basis", "coup"))
    member = lax.axis_index(("basis", "coup"))
    local_count = NB // group
    half_count = local_count // 2
    quarter_count = local_count // 4
    links_local = jnp.concatenate(
        [
            lax.dynamic_slice_in_dim(transfer, member * local_count, local_count, 0),
            lax.dynamic_slice_in_dim(transfer, NB + member * half_count, half_count, 0),
        ],
        axis=0,
    )
    sketch_local = jnp.concatenate(
        [
            lax.dynamic_slice_in_dim(omega, member * local_count, local_count, 0),
            lax.dynamic_slice_in_dim(omega, NB + member * half_count, half_count, 0),
            lax.dynamic_slice_in_dim(
                omega, NB + NB // 2 + member * quarter_count, quarter_count, 0
            ),
        ],
        axis=0,
    )
    local_table = upsweep(gram_share, links_local, sketch_local, local_count)
    collected = lax.all_gather(local_table, ("basis", "coup"), axis=0, tiled=True)
    collected = collected.reshape(group, local_count + half_count + quarter_count, R * K)
    basis_table = jnp.concatenate(
        [
            collected[:, :local_count].reshape(-1, R * K),
            collected[:, local_count : local_count + half_count].reshape(-1, R * K),
            collected[:, local_count + half_count :].reshape(-1, R * K),
        ],
        axis=0,
    )
    slots_per_leaf = basis_table.shape[0]
    left_rows = left_product(basis_table[block_target], blocks)
    local_rows = -(-local_table.shape[0] // 8) * 8
    padded_table = jnp.pad(local_table, ((0, local_rows - local_table.shape[0]), (0, 0)))
    base, node_count = level_slots(block_target)
    within = source_offset % node_count
    per_member = node_count // group
    source_member = source_leaf[:, 0] * group + within // per_member
    source_index = source_member * local_rows + base // group + within % per_member
    gathered = lax.all_gather(padded_table, ("leaf", "basis", "coup"), axis=0, tiled=True)
    source_rows = gathered[source_index]
    return right_product(left_rows, source_rows)


def solution(mesh):
    placed = (
        P("leaf", ("basis", "coup")),
        P("leaf", None),
        P("leaf", None),
        P(("leaf", "basis", "coup"), None),
        P(("leaf", "basis", "coup")),
        P(("leaf", "basis", "coup"), None),
        P(("leaf", "basis", "coup")),
    )
    return jax.shard_map(
        per_device,
        mesh=mesh,
        in_specs=placed,
        out_specs=P(("leaf", "basis", "coup"), None),
        check_vma=False,
    )
```

```python
import jax
import jax.numpy as jnp
from jax import lax
from jax.sharding import PartitionSpec as P
from jax.experimental import pallas as pl
from jax.experimental.pallas import tpu as pltpu

K = 64
R = 32
NB = 64


def level_slots(target):
    base = jnp.where(target < NB, 0, jnp.where(target < NB + NB // 2, NB, NB + NB // 2))
    node_count = jnp.where(target < NB, NB, jnp.where(target < NB + NB // 2, NB // 2, NB // 4))
    return (base, node_count)


def upsweep(gram_bottom, transfer, omega, bottom_count):
    links = transfer.reshape(-1, K, K).astype(jnp.float32)
    levels = [gram_bottom]
    gram_now = gram_bottom
    offset_row = 0
    for node_count in (bottom_count, bottom_count // 2):
        child_links = links[offset_row : offset_row + node_count]
        offset_row = offset_row + node_count
        carried = jnp.einsum(
            "nki,nkl,nlj->nij", child_links, gram_now, child_links, precision=lax.Precision.HIGHEST
        )
        gram_now = carried.reshape(node_count // 2, 2, K, K).sum(axis=1)
        levels.append(gram_now)
    gram_all = jnp.concatenate(levels, axis=0)
    sketch_t = omega.reshape(-1, K, R).astype(jnp.float32).transpose(0, 2, 1)
    basis_table = chol_basis(gram_all, sketch_t)
    return basis_table.astype(jnp.bfloat16).reshape(-1, R * K)


def chol_kernel(g_ref, om_ref, out_ref, lt_ref):
    a = g_ref[...]
    count = a.shape[0]
    lane = lax.broadcasted_iota(jnp.int32, (count, 1, K), 2)
    for j in range(K):
        row = a[:, j : j + 1, :]
        inv = 1.0 / jnp.sqrt(row[:, :, j : j + 1])
        scaled = jnp.where(lane >= j, row * inv, 0.0)
        lt_ref[:, j : j + 1, :] = scaled
        col = a[:, :, j : j + 1] * inv
        a = a - col * scaled
    out_ref[...] = jnp.einsum(
        "nrk,nkj->nrj", om_ref[...], lt_ref[...], precision=lax.Precision.HIGHEST,
        preferred_element_type=jnp.float32,
    )


def chol_basis(gram_all, sketch_t):
    count = gram_all.shape[0]
    return pl.pallas_call(
        chol_kernel,
        out_shape=jax.ShapeDtypeStruct((count, R, K), jnp.float32),
        scratch_shapes=[pltpu.VMEM((count, K, K), jnp.float32)],
    )(gram_all, sketch_t)


def left_kernel(t_ref, s_ref, o_ref):
    tile = t_ref.shape[0]
    target_mat = t_ref[...].reshape(tile, R, K)
    coupling_mat = s_ref[...].reshape(tile, K, K)
    left_prod = jnp.einsum(
        "brk,bkl->brl", target_mat, coupling_mat, preferred_element_type=jnp.float32
    )
    o_ref[...] = left_prod.astype(jnp.bfloat16).reshape(tile, R * K)


def right_kernel(l_ref, src_ref, o_ref):
    tile = l_ref.shape[0]
    left_prod = l_ref[...].reshape(tile, R, K)
    source_mat = src_ref[...].reshape(tile, R, K)
    result = jnp.einsum("brl,bjl->brj", left_prod, source_mat, preferred_element_type=jnp.float32)
    o_ref[...] = result.reshape(tile, R * R)


def row_tiled(kernel, widths, out_width, out_dtype, *arrays):
    count = arrays[0].shape[0]
    tile = 128 if count % 128 == 0 else count
    return pl.pallas_call(
        kernel,
        grid=(count // tile,),
        in_specs=[pl.BlockSpec((tile, w), lambda i: (i, 0)) for w in widths],
        out_specs=pl.BlockSpec((tile, out_width), lambda i: (i, 0)),
        out_shape=jax.ShapeDtypeStruct((count, out_width), out_dtype),
    )(*arrays)


def left_product(target_rows, coupling):
    return row_tiled(left_kernel, (R * K, K * K), R * K, jnp.bfloat16, target_rows, coupling)


def right_product(left_rows, source_rows):
    return row_tiled(right_kernel, (R * K, R * K), R * R, jnp.float32, left_rows, source_rows)


def gram_kernel(x_ref, o_ref):
    tile = x_ref.shape[0]
    rows = x_ref[...].reshape(tile, -1, K)
    o_ref[...] = jnp.einsum("nik,nil->nkl", rows, rows, preferred_element_type=jnp.float32)


def local_gram(basis_rows):
    count, width = basis_rows.shape
    tile = 32 if count % 32 == 0 else count
    return pl.pallas_call(
        gram_kernel,
        grid=(count // tile,),
        in_specs=[pl.BlockSpec((tile, width), lambda i: (i, 0))],
        out_specs=pl.BlockSpec((tile, K, K), lambda i: (i, 0, 0)),
        out_shape=jax.ShapeDtypeStruct((count, K, K), jnp.float32),
    )(basis_rows)


def halving_scatter(x):
    coup_size = lax.axis_size("coup")
    steps = [("basis", 1)] + [("coup", bit) for bit in (2, 1) if bit < coup_size]
    for axis, bit in steps:
        size = lax.axis_size(axis)
        mine = (lax.axis_index(axis) // bit) % 2
        half = x.shape[0] // 2
        keep = lax.dynamic_slice_in_dim(x, mine * half, half, 0)
        send = lax.dynamic_slice_in_dim(x, (1 - mine) * half, half, 0)
        x = keep + lax.ppermute(send, axis, [(i, i ^ bit) for i in range(size)])
    return x


def per_device(basis_rows, transfer, omega, blocks, block_target, source_leaf, source_offset):
    partial_gram = local_gram(basis_rows)
    gram_share = halving_scatter(partial_gram)
    group = lax.axis_size(("basis", "coup"))
    member = lax.axis_index(("basis", "coup"))
    local_count = NB // group
    half_count = local_count // 2
    quarter_count = local_count // 4
    links_local = jnp.concatenate(
        [
            lax.dynamic_slice_in_dim(transfer, member * local_count, local_count, 0),
            lax.dynamic_slice_in_dim(transfer, NB + member * half_count, half_count, 0),
        ],
        axis=0,
    )
    sketch_local = jnp.concatenate(
        [
            lax.dynamic_slice_in_dim(omega, member * local_count, local_count, 0),
            lax.dynamic_slice_in_dim(omega, NB + member * half_count, half_count, 0),
            lax.dynamic_slice_in_dim(
                omega, NB + NB // 2 + member * quarter_count, quarter_count, 0
            ),
        ],
        axis=0,
    )
    local_table = upsweep(gram_share, links_local, sketch_local, local_count)
    collected = lax.all_gather(local_table, ("basis", "coup"), axis=0, tiled=True)
    collected = collected.reshape(group, local_count + half_count + quarter_count, R * K)
    basis_table = jnp.concatenate(
        [
            collected[:, :local_count].reshape(-1, R * K),
            collected[:, local_count : local_count + half_count].reshape(-1, R * K),
            collected[:, local_count + half_count :].reshape(-1, R * K),
        ],
        axis=0,
    )
    slots_per_leaf = basis_table.shape[0]
    left_rows = left_product(basis_table[block_target], blocks)
    local_rows = -(-local_table.shape[0] // 8) * 8
    padded_table = jnp.pad(local_table, ((0, local_rows - local_table.shape[0]), (0, 0)))
    base, node_count = level_slots(block_target)
    within = source_offset % node_count
    per_member = node_count // group
    source_member = source_leaf[:, 0] * group + within // per_member
    source_index = source_member * local_rows + base // group + within % per_member
    gathered = lax.all_gather(padded_table, ("leaf", "basis", "coup"), axis=0, tiled=True)
    source_rows = gathered[source_index]
    return right_product(left_rows, source_rows)


def solution(mesh):
    placed = (
        P("leaf", ("basis", "coup")),
        P("leaf", None),
        P("leaf", None),
        P(("leaf", "basis", "coup"), None),
        P(("leaf", "basis", "coup")),
        P(("leaf", "basis", "coup"), None),
        P(("leaf", "basis", "coup")),
    )
    return jax.shard_map(
        per_device,
        mesh=mesh,
        in_specs=placed,
        out_specs=P(("leaf", "basis", "coup"), None),
        check_vma=False,
    )
```

```python
import jax
import jax.numpy as jnp
from jax import lax
from jax.sharding import PartitionSpec as P
from jax.experimental import pallas as pl
from jax.experimental.pallas import tpu as pltpu

K = 64
R = 32
NB = 64


def level_slots(target):
    base = jnp.where(target < NB, 0, jnp.where(target < NB + NB // 2, NB, NB + NB // 2))
    node_count = jnp.where(target < NB, NB, jnp.where(target < NB + NB // 2, NB // 2, NB // 4))
    return (base, node_count)


def upsweep(gram_bottom, transfer, omega, bottom_count):
    links = transfer.reshape(-1, K, K).astype(jnp.float32)
    levels = [gram_bottom]
    gram_now = gram_bottom
    offset_row = 0
    for node_count in (bottom_count, bottom_count // 2):
        child_links = links[offset_row : offset_row + node_count]
        offset_row = offset_row + node_count
        carried = jnp.einsum(
            "nki,nkl,nlj->nij", child_links, gram_now, child_links, precision=lax.Precision.HIGHEST
        )
        gram_now = carried.reshape(node_count // 2, 2, K, K).sum(axis=1)
        levels.append(gram_now)
    gram_all = jnp.concatenate(levels, axis=0)
    sketch_t = omega.reshape(-1, K, R).astype(jnp.float32).transpose(0, 2, 1)
    basis_table = chol_basis(gram_all, sketch_t)
    return basis_table.astype(jnp.bfloat16).reshape(-1, R * K)


def chol_kernel(g_ref, om_ref, out_ref, lt_ref):
    a = g_ref[...]
    count = a.shape[0]
    lane = lax.broadcasted_iota(jnp.int32, (count, 1, K), 2)
    for j in range(K):
        row = a[:, j : j + 1, :]
        inv = 1.0 / jnp.sqrt(row[:, :, j : j + 1])
        scaled = jnp.where(lane >= j, row * inv, 0.0)
        lt_ref[:, j : j + 1, :] = scaled
        col = a[:, :, j : j + 1] * inv
        a = a - col * scaled
    out_ref[...] = jnp.einsum(
        "nrk,nkj->nrj", om_ref[...], lt_ref[...], precision=lax.Precision.HIGHEST,
        preferred_element_type=jnp.float32,
    )


def chol_basis(gram_all, sketch_t):
    count = gram_all.shape[0]
    return pl.pallas_call(
        chol_kernel,
        out_shape=jax.ShapeDtypeStruct((count, R, K), jnp.float32),
        scratch_shapes=[pltpu.VMEM((count, K, K), jnp.float32)],
    )(gram_all, sketch_t)


def left_kernel(t_ref, s_ref, o_ref):
    tile = t_ref.shape[0]
    target_mat = t_ref[...].reshape(tile, R, K)
    coupling_mat = s_ref[...].reshape(tile, K, K)
    left_prod = jnp.einsum(
        "brk,bkl->brl", target_mat, coupling_mat, preferred_element_type=jnp.float32
    )
    o_ref[...] = left_prod.astype(jnp.bfloat16).reshape(tile, R * K)


def right_kernel(l_ref, src_ref, o_ref):
    tile = l_ref.shape[0]
    left_prod = l_ref[...].reshape(tile, R, K)
    source_mat = src_ref[...].reshape(tile, R, K)
    result = jnp.einsum("brl,bjl->brj", left_prod, source_mat, preferred_element_type=jnp.float32)
    o_ref[...] = result.reshape(tile, R * R)


def row_tiled(kernel, widths, out_width, out_dtype, *arrays):
    count = arrays[0].shape[0]
    tile = 128 if count % 128 == 0 else count
    return pl.pallas_call(
        kernel,
        grid=(count // tile,),
        in_specs=[pl.BlockSpec((tile, w), lambda i: (i, 0)) for w in widths],
        out_specs=pl.BlockSpec((tile, out_width), lambda i: (i, 0)),
        out_shape=jax.ShapeDtypeStruct((count, out_width), out_dtype),
    )(*arrays)


def left_product(target_rows, coupling):
    return row_tiled(left_kernel, (R * K, K * K), R * K, jnp.bfloat16, target_rows, coupling)


def right_product(left_rows, source_rows):
    return row_tiled(right_kernel, (R * K, R * K), R * R, jnp.float32, left_rows, source_rows)


def gram_kernel(x_ref, o_ref):
    tile = x_ref.shape[0]
    rows = x_ref[...].reshape(tile, -1, K)
    gram = jnp.einsum("nik,nil->nkl", rows, rows, preferred_element_type=jnp.float32)
    part = tile // 4
    for c, dst in enumerate((0, 2, 1, 3)):
        o_ref[dst * part : (dst + 1) * part] = gram[c * part : (c + 1) * part]


def local_gram(basis_rows):
    count, width = basis_rows.shape
    tile = 32 if count % 32 == 0 else count
    return pl.pallas_call(
        gram_kernel,
        grid=(count // tile,),
        in_specs=[pl.BlockSpec((tile, width), lambda i: (i, 0))],
        out_specs=pl.BlockSpec((tile, K, K), lambda i: (i, 0, 0)),
        out_shape=jax.ShapeDtypeStruct((count, K, K), jnp.float32),
    )(basis_rows)


def halving_scatter(x):
    coup_size = lax.axis_size("coup")
    steps = [("basis", 1)] + [("coup", bit) for bit in (1, 2) if bit < coup_size]
    for axis, bit in steps:
        size = lax.axis_size(axis)
        mine = (lax.axis_index(axis) // bit) % 2
        half = x.shape[0] // 2
        keep = lax.dynamic_slice_in_dim(x, mine * half, half, 0)
        send = lax.dynamic_slice_in_dim(x, (1 - mine) * half, half, 0)
        x = keep + lax.ppermute(send, axis, [(i, i ^ bit) for i in range(size)])
    return x


def per_device(basis_rows, transfer, omega, blocks, block_target, source_leaf, source_offset):
    partial_gram = local_gram(basis_rows)
    gram_share = halving_scatter(partial_gram)
    group = lax.axis_size(("basis", "coup"))
    member = lax.axis_index(("basis", "coup"))
    local_count = NB // group
    half_count = local_count // 2
    quarter_count = local_count // 4
    links_local = jnp.concatenate(
        [
            lax.dynamic_slice_in_dim(transfer, member * local_count, local_count, 0),
            lax.dynamic_slice_in_dim(transfer, NB + member * half_count, half_count, 0),
        ],
        axis=0,
    )
    sketch_local = jnp.concatenate(
        [
            lax.dynamic_slice_in_dim(omega, member * local_count, local_count, 0),
            lax.dynamic_slice_in_dim(omega, NB + member * half_count, half_count, 0),
            lax.dynamic_slice_in_dim(
                omega, NB + NB // 2 + member * quarter_count, quarter_count, 0
            ),
        ],
        axis=0,
    )
    local_table = upsweep(gram_share, links_local, sketch_local, local_count)
    collected = lax.all_gather(local_table, ("basis", "coup"), axis=0, tiled=True)
    collected = collected.reshape(group, local_count + half_count + quarter_count, R * K)
    basis_table = jnp.concatenate(
        [
            collected[:, :local_count].reshape(-1, R * K),
            collected[:, local_count : local_count + half_count].reshape(-1, R * K),
            collected[:, local_count + half_count :].reshape(-1, R * K),
        ],
        axis=0,
    )
    slots_per_leaf = basis_table.shape[0]
    left_rows = left_product(basis_table[block_target], blocks)
    local_rows = -(-local_table.shape[0] // 8) * 8
    padded_table = jnp.pad(local_table, ((0, local_rows - local_table.shape[0]), (0, 0)))
    base, node_count = level_slots(block_target)
    within = source_offset % node_count
    per_member = node_count // group
    source_member = source_leaf[:, 0] * group + within // per_member
    source_index = source_member * local_rows + base // group + within % per_member
    gathered = lax.all_gather(padded_table, ("leaf", "basis", "coup"), axis=0, tiled=True)
    source_rows = gathered[source_index]
    return right_product(left_rows, source_rows)


def solution(mesh):
    placed = (
        P("leaf", ("basis", "coup")),
        P("leaf", None),
        P("leaf", None),
        P(("leaf", "basis", "coup"), None),
        P(("leaf", "basis", "coup")),
        P(("leaf", "basis", "coup"), None),
        P(("leaf", "basis", "coup")),
    )
    return jax.shard_map(
        per_device,
        mesh=mesh,
        in_specs=placed,
        out_specs=P(("leaf", "basis", "coup"), None),
        check_vma=False,
    )
```

```python
import jax
import jax.numpy as jnp
from jax import lax
from jax.sharding import PartitionSpec as P
from jax.experimental import pallas as pl
from jax.experimental.pallas import tpu as pltpu

K = 64
R = 32
NB = 64


def level_slots(target):
    base = jnp.where(target < NB, 0, jnp.where(target < NB + NB // 2, NB, NB + NB // 2))
    node_count = jnp.where(target < NB, NB, jnp.where(target < NB + NB // 2, NB // 2, NB // 4))
    return (base, node_count)


def upsweep(gram_bottom, transfer, omega, bottom_count):
    links = transfer.reshape(-1, K, K).astype(jnp.float32)
    levels = [gram_bottom]
    gram_now = gram_bottom
    offset_row = 0
    for node_count in (bottom_count, bottom_count // 2):
        child_links = links[offset_row : offset_row + node_count]
        offset_row = offset_row + node_count
        carried = jnp.einsum(
            "nki,nkl,nlj->nij", child_links, gram_now, child_links, precision=lax.Precision.HIGHEST
        )
        gram_now = carried.reshape(node_count // 2, 2, K, K).sum(axis=1)
        levels.append(gram_now)
    gram_all = jnp.concatenate(levels, axis=0)
    sketch_t = omega.reshape(-1, K, R).astype(jnp.float32).transpose(0, 2, 1)
    return chol_basis(gram_all, sketch_t)


def chol_kernel(g_ref, om_ref, out_ref, lt_ref):
    a = g_ref[...]
    count = a.shape[0]
    lane = lax.broadcasted_iota(jnp.int32, (count, 1, K), 2)
    for j in range(K):
        row = a[:, j : j + 1, :]
        inv = 1.0 / jnp.sqrt(row[:, :, j : j + 1])
        scaled = jnp.where(lane >= j, row * inv, 0.0)
        lt_ref[:, j : j + 1, :] = scaled
        col = a[:, :, j : j + 1] * inv
        a = a - col * scaled
    basis = jnp.einsum(
        "nrk,nkj->nrj", om_ref[...], lt_ref[...], precision=lax.Precision.HIGHEST,
        preferred_element_type=jnp.float32,
    )
    out_ref[:count] = basis.astype(jnp.bfloat16).reshape(count, R * K)
    out_ref[count:] = jnp.zeros((out_ref.shape[0] - count, R * K), jnp.bfloat16)


def chol_basis(gram_all, sketch_t):
    count = gram_all.shape[0]
    padded = -(-count // 8) * 8 + (8 if count % 8 == 0 else 0)
    return pl.pallas_call(
        chol_kernel,
        out_shape=jax.ShapeDtypeStruct((padded, R * K), jnp.bfloat16),
        scratch_shapes=[pltpu.VMEM((count, K, K), jnp.float32)],
    )(gram_all, sketch_t)


def left_kernel(t_ref, s_ref, o_ref):
    tile = t_ref.shape[0]
    target_mat = t_ref[...].reshape(tile, R, K)
    coupling_mat = s_ref[...].reshape(tile, K, K)
    left_prod = jnp.einsum(
        "brk,bkl->brl", target_mat, coupling_mat, preferred_element_type=jnp.float32
    )
    o_ref[...] = left_prod.astype(jnp.bfloat16).reshape(tile, R * K)


def right_kernel(l_ref, src_ref, o_ref):
    tile = l_ref.shape[0]
    left_prod = l_ref[...].reshape(tile, R, K)
    source_mat = src_ref[...].reshape(tile, R, K)
    result = jnp.einsum("brl,bjl->brj", left_prod, source_mat, preferred_element_type=jnp.float32)
    o_ref[...] = result.reshape(tile, R * R)


def row_tiled(kernel, widths, out_width, out_dtype, *arrays):
    count = arrays[0].shape[0]
    tile = 128 if count % 128 == 0 else count
    return pl.pallas_call(
        kernel,
        grid=(count // tile,),
        in_specs=[pl.BlockSpec((tile, w), lambda i: (i, 0)) for w in widths],
        out_specs=pl.BlockSpec((tile, out_width), lambda i: (i, 0)),
        out_shape=jax.ShapeDtypeStruct((count, out_width), out_dtype),
    )(*arrays)


def left_product(target_rows, coupling):
    return row_tiled(left_kernel, (R * K, K * K), R * K, jnp.bfloat16, target_rows, coupling)


def right_product(left_rows, source_rows):
    return row_tiled(right_kernel, (R * K, R * K), R * R, jnp.float32, left_rows, source_rows)


def gram_kernel(x_ref, o_ref):
    tile = x_ref.shape[0]
    rows = x_ref[...].reshape(tile, -1, K)
    gram = jnp.einsum("nik,nil->nkl", rows, rows, preferred_element_type=jnp.float32)
    part = tile // 4
    for c, dst in enumerate((0, 2, 1, 3)):
        o_ref[dst * part : (dst + 1) * part] = gram[c * part : (c + 1) * part]


def local_gram(basis_rows):
    count, width = basis_rows.shape
    tile = 32 if count % 32 == 0 else count
    return pl.pallas_call(
        gram_kernel,
        grid=(count // tile,),
        in_specs=[pl.BlockSpec((tile, width), lambda i: (i, 0))],
        out_specs=pl.BlockSpec((tile, K, K), lambda i: (i, 0, 0)),
        out_shape=jax.ShapeDtypeStruct((count, K, K), jnp.float32),
    )(basis_rows)


def halving_scatter(x):
    coup_size = lax.axis_size("coup")
    steps = [("basis", 1)] + [("coup", bit) for bit in (1, 2) if bit < coup_size]
    for axis, bit in steps:
        size = lax.axis_size(axis)
        mine = (lax.axis_index(axis) // bit) % 2
        half = x.shape[0] // 2
        keep = lax.dynamic_slice_in_dim(x, mine * half, half, 0)
        send = lax.dynamic_slice_in_dim(x, (1 - mine) * half, half, 0)
        x = keep + lax.ppermute(send, axis, [(i, i ^ bit) for i in range(size)])
    return x


def per_device(basis_rows, transfer, omega, blocks, block_target, source_leaf, source_offset):
    partial_gram = local_gram(basis_rows)
    gram_share = halving_scatter(partial_gram)
    group = lax.axis_size(("basis", "coup"))
    member = lax.axis_index(("basis", "coup"))
    local_count = NB // group
    half_count = local_count // 2
    quarter_count = local_count // 4
    links_local = jnp.concatenate(
        [
            lax.dynamic_slice_in_dim(transfer, member * local_count, local_count, 0),
            lax.dynamic_slice_in_dim(transfer, NB + member * half_count, half_count, 0),
        ],
        axis=0,
    )
    sketch_local = jnp.concatenate(
        [
            lax.dynamic_slice_in_dim(omega, member * local_count, local_count, 0),
            lax.dynamic_slice_in_dim(omega, NB + member * half_count, half_count, 0),
            lax.dynamic_slice_in_dim(
                omega, NB + NB // 2 + member * quarter_count, quarter_count, 0
            ),
        ],
        axis=0,
    )
    padded_table = upsweep(gram_share, links_local, sketch_local, local_count)
    local_table = padded_table[: local_count + half_count + quarter_count]
    collected = lax.all_gather(local_table, ("basis", "coup"), axis=0, tiled=True)
    collected = collected.reshape(group, local_count + half_count + quarter_count, R * K)
    basis_table = jnp.concatenate(
        [
            collected[:, :local_count].reshape(-1, R * K),
            collected[:, local_count : local_count + half_count].reshape(-1, R * K),
            collected[:, local_count + half_count :].reshape(-1, R * K),
        ],
        axis=0,
    )
    slots_per_leaf = basis_table.shape[0]
    left_rows = left_product(basis_table[block_target], blocks)
    local_rows = padded_table.shape[0]
    base, node_count = level_slots(block_target)
    within = source_offset % node_count
    per_member = node_count // group
    source_member = source_leaf[:, 0] * group + within // per_member
    source_index = source_member * local_rows + base // group + within % per_member
    gathered = lax.all_gather(padded_table, ("leaf", "basis", "coup"), axis=0, tiled=True)
    source_rows = gathered[source_index]
    return right_product(left_rows, source_rows)


def solution(mesh):
    placed = (
        P("leaf", ("basis", "coup")),
        P("leaf", None),
        P("leaf", None),
        P(("leaf", "basis", "coup"), None),
        P(("leaf", "basis", "coup")),
        P(("leaf", "basis", "coup"), None),
        P(("leaf", "basis", "coup")),
    )
    return jax.shard_map(
        per_device,
        mesh=mesh,
        in_specs=placed,
        out_specs=P(("leaf", "basis", "coup"), None),
        check_vma=False,
    )
```

```python
import jax
import jax.numpy as jnp
from jax import lax
from jax.sharding import PartitionSpec as P
from jax.experimental import pallas as pl
from jax.experimental.pallas import tpu as pltpu

K = 64
R = 32
NB = 64


def level_slots(target):
    base = jnp.where(target < NB, 0, jnp.where(target < NB + NB // 2, NB, NB + NB // 2))
    node_count = jnp.where(target < NB, NB, jnp.where(target < NB + NB // 2, NB // 2, NB // 4))
    return (base, node_count)


def upsweep(gram_bottom, transfer, omega, bottom_count):
    links = transfer.reshape(-1, K, K).astype(jnp.float32)
    levels = [gram_bottom]
    gram_now = gram_bottom
    offset_row = 0
    for node_count in (bottom_count, bottom_count // 2):
        child_links = links[offset_row : offset_row + node_count]
        offset_row = offset_row + node_count
        carried = jnp.einsum(
            "nki,nkl,nlj->nij", child_links, gram_now, child_links, precision=lax.Precision.HIGHEST
        )
        gram_now = carried.reshape(node_count // 2, 2, K, K).sum(axis=1)
        levels.append(gram_now)
    gram_all = jnp.concatenate(levels, axis=0)
    sketch_t = omega.reshape(-1, K, R).astype(jnp.float32).transpose(0, 2, 1)
    return chol_basis(gram_all, sketch_t)


def chol_kernel(g_ref, om_ref, out_ref, lt_ref):
    a = g_ref[...]
    count = a.shape[0]
    lane = lax.broadcasted_iota(jnp.int32, (count, 1, K), 2)
    for j in range(K):
        row = a[:, j : j + 1, :]
        inv = 1.0 / jnp.sqrt(row[:, :, j : j + 1])
        scaled = jnp.where(lane >= j, row * inv, 0.0)
        lt_ref[:, j : j + 1, :] = scaled
        col = a[:, :, j : j + 1] * inv
        a = a - col * scaled
    basis = jnp.einsum(
        "nrk,nkj->nrj", om_ref[...], lt_ref[...], precision=lax.Precision.HIGHEST,
        preferred_element_type=jnp.float32,
    )
    out_ref[:count] = basis.astype(jnp.bfloat16).reshape(count, R * K)
    out_ref[count:] = jnp.zeros((out_ref.shape[0] - count, R * K), jnp.bfloat16)


def chol_basis(gram_all, sketch_t):
    count = gram_all.shape[0]
    padded = -(-count // 8) * 8 + (8 if count % 8 == 0 else 0)
    return pl.pallas_call(
        chol_kernel,
        out_shape=jax.ShapeDtypeStruct((padded, R * K), jnp.bfloat16),
        scratch_shapes=[pltpu.VMEM((count, K, K), jnp.float32)],
    )(gram_all, sketch_t)


def left_kernel(t_ref, s_ref, o_ref):
    tile = t_ref.shape[0]
    target_mat = t_ref[...].reshape(tile, R, K)
    coupling_mat = s_ref[...].reshape(tile, K, K)
    left_prod = jnp.einsum(
        "brk,bkl->brl", target_mat, coupling_mat, preferred_element_type=jnp.float32
    )
    o_ref[...] = left_prod.astype(jnp.bfloat16).reshape(tile, R * K)


def right_kernel(l_ref, src_ref, o_ref):
    tile = l_ref.shape[0]
    left_prod = l_ref[...].reshape(tile, R, K)
    source_mat = src_ref[...].reshape(tile, R, K)
    result = jnp.einsum("brl,bjl->brj", left_prod, source_mat, preferred_element_type=jnp.float32)
    o_ref[...] = result.reshape(tile, R * R)


def row_tiled(kernel, widths, out_width, out_dtype, *arrays):
    count = arrays[0].shape[0]
    tile = 128 if count % 128 == 0 else count
    return pl.pallas_call(
        kernel,
        grid=(count // tile,),
        in_specs=[pl.BlockSpec((tile, w), lambda i: (i, 0)) for w in widths],
        out_specs=pl.BlockSpec((tile, out_width), lambda i: (i, 0)),
        out_shape=jax.ShapeDtypeStruct((count, out_width), out_dtype),
    )(*arrays)


def left_product(target_rows, coupling):
    return row_tiled(left_kernel, (R * K, K * K), R * K, jnp.bfloat16, target_rows, coupling)


def right_product(left_rows, source_rows):
    return row_tiled(right_kernel, (R * K, R * K), R * R, jnp.float32, left_rows, source_rows)


def gram_kernel(core_ref, x_ref, o_ref):
    tile = x_ref.shape[0]
    rows = x_ref[...].reshape(tile, -1, K)
    gram = jnp.einsum("nik,nil->nkl", rows, rows, preferred_element_type=jnp.float32)
    part = tile // 4
    for c, dst in enumerate((0, 2, 1, 3)):
        o_ref[dst * part : (dst + 1) * part] = gram[c * part : (c + 1) * part]


def local_gram(basis_rows, core):
    count, width = basis_rows.shape
    tile = count // 2
    return pl.pallas_call(
        gram_kernel,
        grid_spec=pltpu.PrefetchScalarGridSpec(
            num_scalar_prefetch=1,
            grid=(2,),
            in_specs=[pl.BlockSpec((tile, width), lambda i, c: (i, 0))],
            out_specs=pl.BlockSpec((tile, K, K), lambda i, c: ((i + c[0]) % 2, 0, 0)),
        ),
        out_shape=jax.ShapeDtypeStruct((count, K, K), jnp.float32),
    )(core.reshape(1), basis_rows)


def halving_scatter(x):
    coup_size = lax.axis_size("coup")
    half = x.shape[0] // 2
    x = x[:half] + lax.ppermute(x[half:], "basis", [(0, 1), (1, 0)])
    steps = [("coup", bit) for bit in (1, 2) if bit < coup_size]
    for axis, bit in steps:
        size = lax.axis_size(axis)
        mine = (lax.axis_index(axis) // bit) % 2
        half = x.shape[0] // 2
        keep = lax.dynamic_slice_in_dim(x, mine * half, half, 0)
        send = lax.dynamic_slice_in_dim(x, (1 - mine) * half, half, 0)
        x = keep + lax.ppermute(send, axis, [(i, i ^ bit) for i in range(size)])
    return x


def per_device(basis_rows, transfer, omega, blocks, block_target, source_leaf, source_offset):
    partial_gram = local_gram(basis_rows, lax.axis_index("basis").astype(jnp.int32))
    gram_share = halving_scatter(partial_gram)
    group = lax.axis_size(("basis", "coup"))
    member = lax.axis_index(("basis", "coup"))
    local_count = NB // group
    half_count = local_count // 2
    quarter_count = local_count // 4
    links_local = jnp.concatenate(
        [
            lax.dynamic_slice_in_dim(transfer, member * local_count, local_count, 0),
            lax.dynamic_slice_in_dim(transfer, NB + member * half_count, half_count, 0),
        ],
        axis=0,
    )
    sketch_local = jnp.concatenate(
        [
            lax.dynamic_slice_in_dim(omega, member * local_count, local_count, 0),
            lax.dynamic_slice_in_dim(omega, NB + member * half_count, half_count, 0),
            lax.dynamic_slice_in_dim(
                omega, NB + NB // 2 + member * quarter_count, quarter_count, 0
            ),
        ],
        axis=0,
    )
    padded_table = upsweep(gram_share, links_local, sketch_local, local_count)
    local_table = padded_table[: local_count + half_count + quarter_count]
    collected = lax.all_gather(local_table, ("basis", "coup"), axis=0, tiled=True)
    collected = collected.reshape(group, local_count + half_count + quarter_count, R * K)
    basis_table = jnp.concatenate(
        [
            collected[:, :local_count].reshape(-1, R * K),
            collected[:, local_count : local_count + half_count].reshape(-1, R * K),
            collected[:, local_count + half_count :].reshape(-1, R * K),
        ],
        axis=0,
    )
    slots_per_leaf = basis_table.shape[0]
    left_rows = left_product(basis_table[block_target], blocks)
    local_rows = padded_table.shape[0]
    base, node_count = level_slots(block_target)
    within = source_offset % node_count
    per_member = node_count // group
    source_member = source_leaf[:, 0] * group + within // per_member
    source_index = source_member * local_rows + base // group + within % per_member
    gathered = lax.all_gather(padded_table, ("leaf", "basis", "coup"), axis=0, tiled=True)
    source_rows = gathered[source_index]
    return right_product(left_rows, source_rows)


def solution(mesh):
    placed = (
        P("leaf", ("basis", "coup")),
        P("leaf", None),
        P("leaf", None),
        P(("leaf", "basis", "coup"), None),
        P(("leaf", "basis", "coup")),
        P(("leaf", "basis", "coup"), None),
        P(("leaf", "basis", "coup")),
    )
    return jax.shard_map(
        per_device,
        mesh=mesh,
        in_specs=placed,
        out_specs=P(("leaf", "basis", "coup"), None),
        check_vma=False,
    )
```
